512 devices in a mesh: tiles: 128 (over z, y, core), rep: 4 (over x).
Axes of the slice: x: 4, y: 8, z: 8, core: 2. Of those that a mesh axis runs over, the one named last changes fastest.
Arguments:
- tile_data: float32 [1536, 64, 4096], P(('tiles', 'rep')), may hold values from -64 to 64
- tile_coords: int32 [1536, 3], P(('tiles', 'rep')), may hold values from 0 to 127, as said below
- tile_count: int32 [512], P(('tiles', 'rep')), may hold values from 1 to 3, 1024 in all
- weights: int32 [1536], P(('tiles', 'rep')), may hold values from 1 to 4
- owner_map: int32 [128], replicated, may hold values from 0 to 127, as said below
- factor_b: bfloat16 [8192, 256], P(('tiles', 'rep'))
- factor_c: bfloat16 [1024, 256], replicated
Outputs:
- updated: float32 [8192, 256], P(('tiles', 'rep'))
The draws below stay inside these ranges and needn't reach their ends.
Inputs may be any that keep to these rules, and one draw needn't show every extreme that they name: `tile_coords`: columns 0 and 1 name row blocks below 128, column 2 a block below 16. Every slot of device d = t * 4 + e has owner_map[i_s] = t. Among the 3 slots of one device the positions owner_map[j_s] all differ. `owner_map`: A permutation of the 128 row blocks.
All inputs are finite; a program needn't handle non-finite values. No bound on the sum of `tile_count` on one device may be relied on, other than what follows from the above.
Results may differ from the reference program's by a relative error of at most 0.0095.
Values may be sent and summed in bfloat16 or wider, within the bound.
No kernel may reach another device: no remote copies, remote signals or barrier semaphores. Data moves between devices by JAX's collectives and lax.ppermute only.
A program may use at most 128 MiB of HBM per device.

```python
import math
import jax
import jax.numpy as jnp
import numpy as np
from jax import lax

R = 256
TILE = 64
CAP = 3
KB = 16
NB = 128
J = 8192
K = 1024
SLOTS = 1536
LIVE = 1024
DEVICES = 512


def shared_layout(key):
    holders = NB
    devices = SLOTS // CAP
    replicas = devices // holders
    storage = jax.random.permutation(jax.random.fold_in(key, 11), NB)
    inverse = jnp.argsort(storage)
    keys = jax.random.split(jax.random.fold_in(key, 13), devices)

    def single_owner(subkey):
        return jax.random.permutation(subkey, holders)[:CAP]
    second_owner = jax.vmap(single_owner)(keys)
    holder_of = jnp.arange(devices, dtype=jnp.int32) // replicas
    first_block = jnp.broadcast_to(inverse[holder_of][:, None], (devices, CAP))
    second_block = inverse[second_owner]
    third_block = jax.random.randint(jax.random.fold_in(key, 16), (devices, CAP), 0, KB)
    third_block = third_block.at[0, 0].set(KB - 1)
    coords = jnp.stack([first_block, second_block, third_block], -1).reshape(SLOTS, 3)
    return (storage.astype(jnp.int32), coords.astype(jnp.int32))


def draw_tile_coords(key, part):
    return shared_layout(key)[1]


def draw_owner_map(key, part):
    return shared_layout(key)[0]


def factor_values(key, rows):
    unit = jax.random.normal(jax.random.fold_in(key, 1), (rows, R), jnp.float32)
    shared = jax.random.normal(jax.random.fold_in(key, 2), (rows, 1), jnp.float32)
    mixing = 0.5
    low = jnp.log(0.5)
    high = jnp.log(5.0)
    row_scale = jnp.exp(jax.random.uniform(jax.random.fold_in(key, 3), (rows, 1), jnp.float32, low, high))
    rising = 3.0 ** (jnp.arange(rows, dtype=jnp.float32) / rows)
    row_scale = row_scale * rising[:, None]
    col_scale = jnp.exp(jax.random.uniform(jax.random.fold_in(key, 4), (1, R), jnp.float32, low, high))
    values = 0.1 / jnp.sqrt(rows * 1.0) * row_scale * col_scale * (unit + mixing * shared)
    return values.astype(jnp.bfloat16)


def draw_factor_b(key, part):
    return factor_values(jax.random.fold_in(key, 21), J)


def draw_factor_c(key, part):
    return factor_values(jax.random.fold_in(key, 22), K)


def with_ends(array, key, smallest, largest):
    extent = array.shape
    place = [jax.random.randint(jax.random.fold_in(key, axis), (), 0, extent[axis]) for axis in range(len(extent))]
    array = array.at[tuple(place)].set(smallest)
    longest = extent.index(max(extent))
    place[longest] = (place[longest] + 1) % extent[longest]
    return array.at[tuple(place)].set(largest)


def level_of(rng, extent, cuts, least, high):
    def one(dim, shards_of):
        draws = jax.random.uniform(jax.random.fold_in(jax.random.fold_in(rng, 6), dim), (shards_of,), jnp.float32, least / len(cuts), high / len(cuts))
        return jnp.repeat(jnp.exp(draws), extent[dim] // shards_of).reshape((-1,) + (1,) * (len(extent) - dim - 1))

    level = one(*cuts[0])
    for cut in cuts[1:]:
        level = level * one(*cut)
    return level


def length_profile(count, total, bound, lean):
    portions = [(1 << 20) // math.isqrt(standing ** lean) + 1 for standing in range(2, count + 1)]
    rest, counts = total - bound - (count - 1), [1] * (count - 1)
    while rest > 0:
        movable = [i for i in range(count - 1) if counts[i] < bound]
        mass, remaining = sum([portions[i] for i in movable]), rest
        for i in movable:
            more = min(bound - counts[i], max(1, remaining * portions[i] // mass), rest)
            counts[i] = counts[i] + more
            rest = rest - more
    return np.array([bound] + counts)


def ragged_sizes(own_key, count, total, limit, lean):
    if count == 2:
        one = jax.random.randint(own_key, (), max(1, total - limit), min(limit, total - 1) + 1)
        return jnp.stack([one, total - one])
    sizes = jnp.asarray(length_profile(count, total, limit, lean), jnp.int32)
    pairs = (count - 1) // 2
    giver, receiver = sizes[1:1 + 2 * pairs:2], sizes[2:2 + 2 * pairs:2]
    margin = jnp.minimum(giver - 1, limit - receiver)
    passed = jax.random.randint(jax.random.fold_in(own_key, 1), (pairs,), 0, 1 << 20) % (margin + 1)
    sizes = sizes.at[1:1 + 2 * pairs:2].set(giver - passed).at[2:2 + 2 * pairs:2].set(receiver + passed)
    return sizes[jax.random.permutation(jax.random.fold_in(own_key, 2), count)]


def bell_draw(key, shape, width, bound, cuts=(), held_as=jnp.bfloat16):
    array = width * jax.random.normal(key, shape, jnp.float32)
    if cuts:
        array = array * level_of(key, shape, cuts, -0.22, 0.18)
    return jnp.clip(array, -bound, bound).astype(held_as)


def setup_inputs(seed: int = 0) -> dict:
    splits = jax.random.split(jax.random.key(seed), 8)
    tile_data = bell_draw(splits[0], (SLOTS, TILE, TILE * TILE), ((J * K) ** 0.5 / (4 * TILE)), 64.0, ((0, 512),), jnp.float32)
    tile_coords = draw_tile_coords(jax.random.fold_in(splits[7], 71), 0)
    tile_count = ragged_sizes(splits[2], DEVICES, LIVE, CAP, 2).astype(jnp.int32)
    weights = with_ends(jax.random.randint(splits[3], (SLOTS,), 1, 5), jax.random.fold_in(splits[3], 1), 1, 4).astype(jnp.int32)
    owner_map = draw_owner_map(jax.random.fold_in(splits[7], 71), 0)
    factor_b = draw_factor_b(jax.random.fold_in(splits[7], 71), 0)
    factor_c = draw_factor_c(jax.random.fold_in(splits[7], 71), 0)
    return dict(tile_data=tile_data, tile_coords=tile_coords, tile_count=tile_count, weights=weights, owner_map=owner_map, factor_b=factor_b, factor_c=factor_c)


def reference(tile_data, tile_coords, tile_count, weights, owner_map, factor_b, factor_c):
    slot_total = tile_data.shape[0]
    position = jnp.arange(slot_total, dtype=jnp.int32)
    is_live = position % CAP < jnp.repeat(tile_count, CAP)
    slot_scale = weights.astype(jnp.float32) * is_live.astype(jnp.float32)

    def one_tile(packed):
        single, coords_row, factor_weight = packed
        stored = owner_map[coords_row[1]]
        b_block = lax.dynamic_slice_in_dim(factor_b, (stored * TILE).astype(jnp.int32), TILE, 0).astype(jnp.float32)
        c_block = lax.dynamic_slice_in_dim(factor_c, (coords_row[2] * TILE).astype(jnp.int32), TILE, 0).astype(jnp.float32)
        inner_sum = jnp.dot(single.reshape(TILE * TILE, TILE), c_block, precision=lax.Precision.HIGHEST)
        inner_sum = inner_sum.reshape(TILE, TILE, R)
        partial_value = jnp.einsum('ijr,jr->ir', inner_sum, b_block)
        return (partial_value * factor_weight).astype(jnp.bfloat16)
    contribution = lax.map(one_tile, (tile_data, tile_coords, slot_scale))
    mttkrp = jax.ops.segment_sum(contribution.astype(jnp.float32), tile_coords[:, 0], num_segments=NB)
    gram_b = jnp.dot(factor_b.T.astype(jnp.float32), factor_b.astype(jnp.float32), preferred_element_type=jnp.float32)
    gram_c = jnp.dot(factor_c.T.astype(jnp.float32), factor_c.astype(jnp.float32), preferred_element_type=jnp.float32)
    normal_matrix = gram_b * gram_c
    lower_factor = jnp.linalg.cholesky(normal_matrix)
    solved = jax.scipy.linalg.cho_solve((lower_factor, True), mttkrp.reshape(NB * TILE, R).T).T
    stored_blocks = jnp.zeros((NB, TILE, R), jnp.float32).at[owner_map].set(solved.reshape(NB, TILE, R))
    return stored_blocks.reshape(NB * TILE, R)
```

```python
import jax
import jax.numpy as jnp
from jax import lax
from jax.sharding import PartitionSpec as P


def per_device(tile_data, tile_coords, tile_count, weights, owner_map, factor_b, factor_c):
    slot_total = tile_data.shape[0]
    tile_edge = tile_data.shape[1]
    rank_cols = factor_b.shape[1]
    is_live = jnp.arange(slot_total, dtype=jnp.int32) < tile_count[0]
    slot_scale = weights.astype(jnp.float32) * is_live.astype(jnp.float32)
    stored_second = jnp.take(owner_map, tile_coords[:, 1])
    owned = lax.all_gather(factor_b, "rep", axis=0, tiled=True)
    whole_b = lax.all_gather(owned, "tiles", axis=0, tiled=True)
    summed = jnp.zeros((tile_edge, rank_cols), jnp.float32)
    for position in range(slot_total):
        c_block = lax.dynamic_slice_in_dim(
            factor_c, tile_coords[position, 2] * tile_edge, tile_edge, 0
        ).astype(jnp.float32)
        b_block = lax.dynamic_slice_in_dim(
            whole_b, stored_second[position] * tile_edge, tile_edge, 0
        ).astype(jnp.float32)
        flat_tile = tile_data[position].reshape(tile_edge * tile_edge, tile_edge)
        inner_sum = jnp.dot(flat_tile, c_block, precision=lax.Precision.HIGHEST)
        inner_sum = inner_sum.reshape(tile_edge, tile_edge, rank_cols)
        partial_value = jnp.einsum("ijr,jr->ir", inner_sum, b_block)
        rounded = (partial_value * slot_scale[position]).astype(jnp.bfloat16)
        summed = summed + rounded.astype(jnp.float32)
    my_rows = lax.psum_scatter(summed, "rep", scatter_dimension=0, tiled=True)
    gram_b = jnp.dot(whole_b.T, whole_b, preferred_element_type=jnp.float32)
    gram_c = jnp.dot(factor_c.T, factor_c, preferred_element_type=jnp.float32)
    normal_matrix = gram_b * gram_c
    lower_factor = jnp.linalg.cholesky(normal_matrix)
    return jax.scipy.linalg.cho_solve((lower_factor, True), my_rows.T).T


def solution(mesh):
    in_specs = (
        P(("tiles", "rep"), None, None),
        P(("tiles", "rep"), None),
        P(("tiles", "rep")),
        P(("tiles", "rep")),
        P(),
        P(("tiles", "rep"), None),
        P(),
    )
    out_specs = P(("tiles", "rep"), None)
    return jax.shard_map(
        per_device, mesh=mesh, in_specs=in_specs, out_specs=out_specs, check_vma=False
    )
```

```python
import jax
import jax.numpy as jnp
from jax import lax
from jax.sharding import PartitionSpec as P


def per_device(tile_data, tile_coords, tile_count, weights, owner_map, factor_b, factor_c):
    slot_total = tile_data.shape[0]
    tile_edge = tile_data.shape[1]
    rank_cols = factor_b.shape[1]
    is_live = jnp.arange(slot_total, dtype=jnp.int32) < tile_count[0]
    slot_scale = weights.astype(jnp.float32) * is_live.astype(jnp.float32)
    stored_second = jnp.take(owner_map, tile_coords[:, 1])
    owned = lax.all_gather(factor_b, "rep", axis=0, tiled=True)
    whole_b = lax.all_gather(owned, "tiles", axis=0, tiled=True)
    summed = jnp.zeros((tile_edge, rank_cols), jnp.float32)
    for position in range(slot_total):
        c_block = lax.dynamic_slice_in_dim(
            factor_c, tile_coords[position, 2] * tile_edge, tile_edge, 0
        ).astype(jnp.float32)
        b_block = lax.dynamic_slice_in_dim(
            whole_b, stored_second[position] * tile_edge, tile_edge, 0
        ).astype(jnp.float32)
        flat_tile = tile_data[position].reshape(tile_edge * tile_edge, tile_edge)
        inner_sum = jnp.dot(flat_tile, c_block, precision=lax.Precision.HIGHEST)
        inner_sum = inner_sum.reshape(tile_edge, tile_edge, rank_cols)
        partial_value = jnp.einsum("ijr,jr->ir", inner_sum, b_block)
        rounded = (partial_value * slot_scale[position]).astype(jnp.bfloat16)
        summed = summed + rounded.astype(jnp.float32)
    summed, whole_b = lax.optimization_barrier((summed, whole_b))
    my_rows = lax.psum_scatter(summed, "rep", scatter_dimension=0, tiled=True)
    gram_b = jnp.dot(whole_b.T, whole_b, preferred_element_type=jnp.float32)
    gram_c = jnp.dot(factor_c.T, factor_c, preferred_element_type=jnp.float32)
    normal_matrix = gram_b * gram_c
    lower_factor = jnp.linalg.cholesky(normal_matrix)
    identity = jnp.eye(rank_cols, dtype=jnp.float32)
    lower_inverse = lax.linalg.triangular_solve(
        lower_factor, identity, left_side=True, lower=True
    )
    normal_inverse = jnp.dot(
        lower_inverse.T, lower_inverse, precision=lax.Precision.HIGHEST
    )
    return jnp.dot(my_rows, normal_inverse, precision=lax.Precision.HIGHEST)


def solution(mesh):
    in_specs = (
        P(("tiles", "rep"), None, None),
        P(("tiles", "rep"), None),
        P(("tiles", "rep")),
        P(("tiles", "rep")),
        P(),
        P(("tiles", "rep"), None),
        P(),
    )
    out_specs = P(("tiles", "rep"), None)
    return jax.shard_map(
        per_device, mesh=mesh, in_specs=in_specs, out_specs=out_specs, check_vma=False
    )
```

```python
import jax
import jax.numpy as jnp
from jax import lax
from jax.sharding import PartitionSpec as P


def per_device(tile_data, tile_coords, tile_count, weights, owner_map, factor_b, factor_c):
    slot_total = tile_data.shape[0]
    tile_edge = tile_data.shape[1]
    rank_cols = factor_b.shape[1]
    is_live = jnp.arange(slot_total, dtype=jnp.int32) < tile_count[0]
    slot_scale = weights.astype(jnp.float32) * is_live.astype(jnp.float32)
    stored_second = jnp.take(owner_map, tile_coords[:, 1])
    owned = lax.all_gather(factor_b, "rep", axis=0, tiled=True)
    whole_b = lax.all_gather(owned, "tiles", axis=0, tiled=True)
    summed = jnp.zeros((tile_edge, rank_cols), jnp.float32)
    for position in range(slot_total):
        c_block = lax.dynamic_slice_in_dim(
            factor_c, tile_coords[position, 2] * tile_edge, tile_edge, 0
        ).astype(jnp.float32)
        b_block = lax.dynamic_slice_in_dim(
            whole_b, stored_second[position] * tile_edge, tile_edge, 0
        ).astype(jnp.float32)
        flat_tile = tile_data[position].reshape(tile_edge * tile_edge, tile_edge)
        inner_sum = jnp.dot(flat_tile, c_block, precision=lax.Precision.HIGHEST)
        inner_sum = inner_sum.reshape(tile_edge, tile_edge, rank_cols)
        partial_value = jnp.einsum("ijr,jr->ir", inner_sum, b_block)
        rounded = (partial_value * slot_scale[position]).astype(jnp.bfloat16)
        summed = summed + rounded.astype(jnp.float32)
    summed, whole_b = lax.optimization_barrier((summed, whole_b))
    my_rows = lax.psum_scatter(summed, "rep", scatter_dimension=0, tiled=True)
    gram_b = jnp.dot(whole_b.T, whole_b, preferred_element_type=jnp.float32)
    gram_c = jnp.dot(factor_c.T, factor_c, preferred_element_type=jnp.float32)
    normal_matrix = gram_b * gram_c
    normal_inverse = spd_inverse(normal_matrix)
    return jnp.dot(my_rows, normal_inverse, precision=lax.Precision.HIGHEST)


def mm(left, right):
    return jnp.dot(left, right, precision=lax.Precision.HIGHEST)


def lower_inverse(lower):
    size = lower.shape[0]
    diagonal = jnp.diagonal(lower)
    identity = jnp.eye(size, dtype=lower.dtype)
    strict = identity - lower / diagonal[:, None]
    product = identity + strict
    power = strict
    reach = 2
    while reach < size:
        power = mm(power, power)
        product = product + mm(product, power)
        reach *= 2
    return product / diagonal[None, :]


def spd_inverse(matrix):
    half = matrix.shape[0] // 2
    top = matrix[:half, :half]
    side = matrix[half:, :half]
    bottom = matrix[half:, half:]
    top_inverse = lower_inverse(lax.linalg.cholesky(top))
    side_factor = mm(side, top_inverse.T)
    schur = bottom - mm(side_factor, side_factor.T)
    bottom_inverse = lower_inverse(lax.linalg.cholesky(schur))
    corner = -mm(bottom_inverse, mm(side_factor, top_inverse))
    zeros = jnp.zeros((half, matrix.shape[0] - half), matrix.dtype)
    inverse = jnp.concatenate(
        [jnp.concatenate([top_inverse, zeros], 1), jnp.concatenate([corner, bottom_inverse], 1)], 0
    )
    return mm(inverse.T, inverse)


def solution(mesh):
    in_specs = (
        P(("tiles", "rep"), None, None),
        P(("tiles", "rep"), None),
        P(("tiles", "rep")),
        P(("tiles", "rep")),
        P(),
        P(("tiles", "rep"), None),
        P(),
    )
    out_specs = P(("tiles", "rep"), None)
    return jax.shard_map(
        per_device, mesh=mesh, in_specs=in_specs, out_specs=out_specs, check_vma=False
    )
```

```python
import jax
import jax.numpy as jnp
from jax import lax
from jax.sharding import PartitionSpec as P


def per_device(tile_data, tile_coords, tile_count, weights, owner_map, factor_b, factor_c):
    slot_total = tile_data.shape[0]
    tile_edge = tile_data.shape[1]
    rank_cols = factor_b.shape[1]
    is_live = jnp.arange(slot_total, dtype=jnp.int32) < tile_count[0]
    slot_scale = weights.astype(jnp.float32) * is_live.astype(jnp.float32)
    stored_second = jnp.take(owner_map, tile_coords[:, 1])
    replicas = lax.psum(1, "rep")
    mine = lax.axis_index("rep")
    by_shift = [factor_b] + [
        lax.ppermute(factor_b, "rep", [(e, (e + k) % replicas) for e in range(replicas)])
        for k in range(1, replicas)
    ]
    order = (mine - jnp.arange(replicas)) % replicas
    owned = jnp.take(jnp.stack(by_shift), order, axis=0).reshape(-1, rank_cols)
    whole_b = lax.all_gather(owned, "tiles", axis=0, tiled=True)
    summed = jnp.zeros((tile_edge, rank_cols), jnp.float32)
    for position in range(slot_total):
        c_block = lax.dynamic_slice_in_dim(
            factor_c, tile_coords[position, 2] * tile_edge, tile_edge, 0
        ).astype(jnp.float32)
        b_block = lax.dynamic_slice_in_dim(
            whole_b, stored_second[position] * tile_edge, tile_edge, 0
        ).astype(jnp.float32)
        flat_tile = tile_data[position].reshape(tile_edge * tile_edge, tile_edge)
        inner_sum = jnp.dot(flat_tile, c_block, precision=lax.Precision.HIGHEST)
        inner_sum = inner_sum.reshape(tile_edge, tile_edge, rank_cols)
        partial_value = jnp.einsum("ijr,jr->ir", inner_sum, b_block)
        rounded = (partial_value * slot_scale[position]).astype(jnp.bfloat16)
        summed = summed + rounded.astype(jnp.float32)
    summed, whole_b = lax.optimization_barrier((summed, whole_b))
    share = tile_edge // replicas
    my_rows = lax.dynamic_slice_in_dim(summed, mine * share, share, 0)
    for k in range(1, replicas):
        outgoing = lax.dynamic_slice_in_dim(summed, ((mine + k) % replicas) * share, share, 0)
        my_rows = my_rows + lax.ppermute(
            outgoing, "rep", [(e, (e + k) % replicas) for e in range(replicas)]
        )
    gram_b = jnp.dot(whole_b.T, whole_b, preferred_element_type=jnp.float32)
    gram_c = jnp.dot(factor_c.T, factor_c, preferred_element_type=jnp.float32)
    normal_matrix = gram_b * gram_c
    normal_inverse, my_rows = spd_inverse(normal_matrix, my_rows)
    return jnp.dot(my_rows, normal_inverse, precision=lax.Precision.HIGHEST)


def mm(left, right):
    return jnp.dot(left, right, precision=lax.Precision.HIGHEST)


def lower_inverse(lower):
    size = lower.shape[0]
    diagonal = jnp.diagonal(lower)
    identity = jnp.eye(size, dtype=lower.dtype)
    strict = identity - lower / diagonal[:, None]
    product = identity + strict
    power = strict
    reach = 2
    while reach < size:
        power = mm(power, power)
        product = product + mm(product, power)
        reach *= 2
    return product / diagonal[None, :]


def spd_inverse(matrix, carried):
    half = matrix.shape[0] // 2
    top = matrix[:half, :half]
    side = matrix[half:, :half]
    bottom = matrix[half:, half:]
    top_inverse = lower_inverse(lax.linalg.cholesky(top))
    side_factor = mm(side, top_inverse.T)
    schur = bottom - mm(side_factor, side_factor.T)
    schur, carried = lax.optimization_barrier((schur, carried))
    bottom_inverse = lower_inverse(lax.linalg.cholesky(schur))
    corner = -mm(bottom_inverse, mm(side_factor, top_inverse))
    zeros = jnp.zeros((half, matrix.shape[0] - half), matrix.dtype)
    inverse = jnp.concatenate(
        [jnp.concatenate([top_inverse, zeros], 1), jnp.concatenate([corner, bottom_inverse], 1)], 0
    )
    return mm(inverse.T, inverse), carried


def solution(mesh):
    in_specs = (
        P(("tiles", "rep"), None, None),
        P(("tiles", "rep"), None),
        P(("tiles", "rep")),
        P(("tiles", "rep")),
        P(),
        P(("tiles", "rep"), None),
        P(),
    )
    out_specs = P(("tiles", "rep"), None)
    return jax.shard_map(
        per_device, mesh=mesh, in_specs=in_specs, out_specs=out_specs, check_vma=False
    )
```

```python
import jax
import jax.numpy as jnp
from jax import lax
from jax.sharding import PartitionSpec as P


def per_device(tile_data, tile_coords, tile_count, weights, owner_map, factor_b, factor_c):
    slot_total = tile_data.shape[0]
    tile_edge = tile_data.shape[1]
    rank_cols = factor_b.shape[1]
    is_live = jnp.arange(slot_total, dtype=jnp.int32) < tile_count[0]
    slot_scale = weights.astype(jnp.float32) * is_live.astype(jnp.float32)
    stored_second = jnp.take(owner_map, tile_coords[:, 1])
    replicas = lax.psum(1, "rep")
    mine = lax.axis_index("rep")
    by_shift = [factor_b] + [
        lax.ppermute(factor_b, "rep", [(e, (e + k) % replicas) for e in range(replicas)])
        for k in range(1, replicas)
    ]
    order = (mine - jnp.arange(replicas)) % replicas
    owned = jnp.take(jnp.stack(by_shift), order, axis=0).reshape(-1, rank_cols)
    holders = lax.psum(1, "tiles")
    me = lax.axis_index("tiles")
    levels = holders.bit_length() - 1
    gathered = owned[None]
    for bit in reversed(range(levels)):
        partner = [(t, t ^ (1 << bit)) for t in range(holders)]
        gathered = jnp.concatenate([gathered, lax.ppermute(gathered, "tiles", partner)], 0)
    whole_b = gathered.reshape(-1, rank_cols)
    apart = stored_second ^ me
    place = sum(((apart >> (levels - 1 - k)) & 1) << k for k in range(levels))
    summed = jnp.zeros((tile_edge, rank_cols), jnp.float32)
    for position in range(slot_total):
        c_block = lax.dynamic_slice_in_dim(
            factor_c, tile_coords[position, 2] * tile_edge, tile_edge, 0
        ).astype(jnp.float32)
        b_block = lax.dynamic_slice_in_dim(
            whole_b, place[position] * tile_edge, tile_edge, 0
        ).astype(jnp.float32)
        flat_tile = tile_data[position].reshape(tile_edge * tile_edge, tile_edge)
        inner_sum = jnp.dot(flat_tile, c_block, precision=lax.Precision.HIGHEST)
        inner_sum = inner_sum.reshape(tile_edge, tile_edge, rank_cols)
        partial_value = jnp.einsum("ijr,jr->ir", inner_sum, b_block)
        rounded = (partial_value * slot_scale[position]).astype(jnp.bfloat16)
        summed = summed + rounded.astype(jnp.float32)
    summed, whole_b = lax.optimization_barrier((summed, whole_b))
    share = tile_edge // replicas
    my_rows = lax.dynamic_slice_in_dim(summed, mine * share, share, 0)
    for k in range(1, replicas):
        outgoing = lax.dynamic_slice_in_dim(summed, ((mine + k) % replicas) * share, share, 0)
        my_rows = my_rows + lax.ppermute(
            outgoing, "rep", [(e, (e + k) % replicas) for e in range(replicas)]
        )
    gram_b = jnp.dot(whole_b.T, whole_b, preferred_element_type=jnp.float32)
    gram_c = jnp.dot(factor_c.T, factor_c, preferred_element_type=jnp.float32)
    normal_matrix = gram_b * gram_c
    normal_inverse, my_rows = spd_inverse(normal_matrix, my_rows)
    return jnp.dot(my_rows, normal_inverse, precision=lax.Precision.HIGHEST)


def mm(left, right):
    return jnp.dot(left, right, precision=lax.Precision.HIGHEST)


def lower_inverse(lower):
    size = lower.shape[0]
    diagonal = jnp.diagonal(lower)
    identity = jnp.eye(size, dtype=lower.dtype)
    strict = identity - lower / diagonal[:, None]
    product = identity + strict
    power = strict
    reach = 2
    while reach < size:
        power = mm(power, power)
        product = product + mm(product, power)
        reach *= 2
    return product / diagonal[None, :]


def spd_inverse(matrix, carried):
    half = matrix.shape[0] // 2
    top = matrix[:half, :half]
    side = matrix[half:, :half]
    bottom = matrix[half:, half:]
    top_inverse = lower_inverse(lax.linalg.cholesky(top))
    side_factor = mm(side, top_inverse.T)
    schur = bottom - mm(side_factor, side_factor.T)
    schur, carried = lax.optimization_barrier((schur, carried))
    bottom_inverse = lower_inverse(lax.linalg.cholesky(schur))
    corner = -mm(bottom_inverse, mm(side_factor, top_inverse))
    zeros = jnp.zeros((half, matrix.shape[0] - half), matrix.dtype)
    inverse = jnp.concatenate(
        [jnp.concatenate([top_inverse, zeros], 1), jnp.concatenate([corner, bottom_inverse], 1)], 0
    )
    return mm(inverse.T, inverse), carried


def solution(mesh):
    in_specs = (
        P(("tiles", "rep"), None, None),
        P(("tiles", "rep"), None),
        P(("tiles", "rep")),
        P(("tiles", "rep")),
        P(),
        P(("tiles", "rep"), None),
        P(),
    )
    out_specs = P(("tiles", "rep"), None)
    return jax.shard_map(
        per_device, mesh=mesh, in_specs=in_specs, out_specs=out_specs, check_vma=False
    )
```

```python
import jax
import jax.numpy as jnp
from jax import lax
from jax.sharding import PartitionSpec as P


def per_device(tile_data, tile_coords, tile_count, weights, owner_map, factor_b, factor_c):
    slot_total = tile_data.shape[0]
    tile_edge = tile_data.shape[1]
    rank_cols = factor_b.shape[1]
    is_live = jnp.arange(slot_total, dtype=jnp.int32) < tile_count[0]
    slot_scale = weights.astype(jnp.float32) * is_live.astype(jnp.float32)
    stored_second = jnp.take(owner_map, tile_coords[:, 1])
    replicas = lax.psum(1, "rep")
    copies = jnp.broadcast_to(factor_b[None], (replicas,) + factor_b.shape)
    owned = lax.all_to_all(copies, "rep", 0, 0).reshape(-1, rank_cols)
    whole_b = lax.all_gather(owned, "tiles", axis=0, tiled=True)
    summed = jnp.zeros((tile_edge, rank_cols), jnp.float32)
    for position in range(slot_total):
        c_block = lax.dynamic_slice_in_dim(
            factor_c, tile_coords[position, 2] * tile_edge, tile_edge, 0
        ).astype(jnp.float32)
        b_block = lax.dynamic_slice_in_dim(
            whole_b, stored_second[position] * tile_edge, tile_edge, 0
        ).astype(jnp.float32)
        flat_tile = tile_data[position].reshape(tile_edge * tile_edge, tile_edge)
        inner_sum = jnp.dot(flat_tile, c_block, precision=lax.Precision.HIGHEST)
        inner_sum = inner_sum.reshape(tile_edge, tile_edge, rank_cols)
        partial_value = jnp.einsum("ijr,jr->ir", inner_sum, b_block)
        rounded = (partial_value * slot_scale[position]).astype(jnp.bfloat16)
        summed = summed + rounded.astype(jnp.float32)
    summed, whole_b = lax.optimization_barrier((summed, whole_b))
    pieces = summed.reshape(replicas, tile_edge // replicas, rank_cols)
    my_rows = lax.all_to_all(pieces, "rep", 0, 0).sum(0)
    gram_b = jnp.dot(whole_b.T, whole_b, preferred_element_type=jnp.float32)
    gram_c = jnp.dot(factor_c.T, factor_c, preferred_element_type=jnp.float32)
    normal_matrix = gram_b * gram_c
    normal_inverse, my_rows = spd_inverse(normal_matrix, my_rows)
    return jnp.dot(my_rows, normal_inverse, precision=lax.Precision.HIGHEST)


def mm(left, right):
    return jnp.dot(left, right, precision=lax.Precision.HIGHEST)


def lower_inverse(lower):
    size = lower.shape[0]
    diagonal = jnp.diagonal(lower)
    identity = jnp.eye(size, dtype=lower.dtype)
    strict = identity - lower / diagonal[:, None]
    product = identity + strict
    power = strict
    reach = 2
    while reach < size:
        power = mm(power, power)
        product = product + mm(product, power)
        reach *= 2
    return product / diagonal[None, :]


def spd_inverse(matrix, carried):
    half = matrix.shape[0] // 2
    top = matrix[:half, :half]
    side = matrix[half:, :half]
    bottom = matrix[half:, half:]
    top_inverse = lower_inverse(lax.linalg.cholesky(top))
    side_factor = mm(side, top_inverse.T)
    schur = bottom - mm(side_factor, side_factor.T)
    schur, carried = lax.optimization_barrier((schur, carried))
    bottom_inverse = lower_inverse(lax.linalg.cholesky(schur))
    corner = -mm(bottom_inverse, mm(side_factor, top_inverse))
    zeros = jnp.zeros((half, matrix.shape[0] - half), matrix.dtype)
    inverse = jnp.concatenate(
        [jnp.concatenate([top_inverse, zeros], 1), jnp.concatenate([corner, bottom_inverse], 1)], 0
    )
    return mm(inverse.T, inverse), carried


def solution(mesh):
    in_specs = (
        P(("tiles", "rep"), None, None),
        P(("tiles", "rep"), None),
        P(("tiles", "rep")),
        P(("tiles", "rep")),
        P(),
        P(("tiles", "rep"), None),
        P(),
    )
    out_specs = P(("tiles", "rep"), None)
    return jax.shard_map(
        per_device, mesh=mesh, in_specs=in_specs, out_specs=out_specs, check_vma=False
    )
```

```python
import jax
import jax.numpy as jnp
from jax import lax
from jax.experimental import pallas as pl
from jax.experimental.pallas import tpu as pltpu
from jax.sharding import PartitionSpec as P


def per_device(tile_data, tile_coords, tile_count, weights, owner_map, factor_b, factor_c):
    slot_total = tile_data.shape[0]
    tile_edge = tile_data.shape[1]
    rank_cols = factor_b.shape[1]
    is_live = jnp.arange(slot_total, dtype=jnp.int32) < tile_count[0]
    slot_scale = weights.astype(jnp.float32) * is_live.astype(jnp.float32)
    stored_second = jnp.take(owner_map, tile_coords[:, 1])
    replicas = lax.psum(1, "rep")
    copies = jnp.broadcast_to(factor_b[None], (replicas,) + factor_b.shape)
    owned = lax.all_to_all(copies, "rep", 0, 0).reshape(-1, rank_cols)
    whole_b = lax.all_gather(owned, "tiles", axis=0, tiled=True)
    inners = []
    b_blocks = []
    for position in range(slot_total):
        c_block = lax.dynamic_slice_in_dim(
            factor_c, tile_coords[position, 2] * tile_edge, tile_edge, 0
        ).astype(jnp.float32)
        b_blocks.append(
            lax.dynamic_slice_in_dim(whole_b, stored_second[position] * tile_edge, tile_edge, 0)
        )
        flat_tile = tile_data[position].reshape(tile_edge * tile_edge, tile_edge)
        inner_sum = jnp.dot(flat_tile, c_block, precision=lax.Precision.HIGHEST)
        inners.append(inner_sum.reshape(tile_edge, tile_edge, rank_cols))
    summed = weighted_sum(slot_scale, jnp.stack(b_blocks), inners)
    summed, whole_b = lax.optimization_barrier((summed, whole_b))
    pieces = summed.reshape(replicas, tile_edge // replicas, rank_cols)
    my_rows = lax.all_to_all(pieces, "rep", 0, 0).sum(0)
    gram_b = jnp.dot(whole_b.T, whole_b, preferred_element_type=jnp.float32)
    gram_c = jnp.dot(factor_c.T, factor_c, preferred_element_type=jnp.float32)
    normal_matrix = gram_b * gram_c
    normal_inverse, my_rows = spd_inverse(normal_matrix, my_rows)
    return jnp.dot(my_rows, normal_inverse, precision=lax.Precision.HIGHEST)


def weigh_kernel(scale_ref, b_ref, *refs):
    inner_refs, out_ref = refs[:-1], refs[-1]
    total = jnp.zeros(out_ref.shape, jnp.float32)
    for slot, inner_ref in enumerate(inner_refs):
        second = b_ref[slot].astype(jnp.float32)
        partial_value = jnp.sum(inner_ref[...] * second[None], axis=1)
        rounded = (partial_value * scale_ref[slot]).astype(jnp.bfloat16)
        total = total + rounded.astype(jnp.float32)
    out_ref[...] = total


def weighted_sum(slot_scale, b_blocks, inners, rows=8):
    edge, second, rank_cols = inners[0].shape
    inner_spec = pl.BlockSpec((rows, second, rank_cols), lambda i: (i, 0, 0))
    return pl.pallas_call(
        weigh_kernel,
        grid=(edge // rows,),
        in_specs=[
            pl.BlockSpec(memory_space=pltpu.SMEM),
            pl.BlockSpec(b_blocks.shape, lambda i: (0, 0, 0)),
        ]
        + [inner_spec] * len(inners),
        out_specs=pl.BlockSpec((rows, rank_cols), lambda i: (i, 0)),
        out_shape=jax.ShapeDtypeStruct((edge, rank_cols), jnp.float32),
    )(slot_scale, b_blocks, *inners)


def mm(left, right):
    return jnp.dot(left, right, precision=lax.Precision.HIGHEST)


def lower_inverse(lower):
    size = lower.shape[0]
    identity = jnp.eye(size, dtype=lower.dtype)
    diagonal = jnp.sum(lower * identity, axis=1)
    strict = identity - lower / diagonal[:, None]
    product = identity + strict
    power = strict
    reach = 2
    while reach < size:
        power = mm(power, power)
        product = product + mm(product, power)
        reach *= 2
    return product / diagonal[None, :]


def spd_inverse(matrix, carried):
    half = matrix.shape[0] // 2
    top = matrix[:half, :half]
    side = matrix[half:, :half]
    bottom = matrix[half:, half:]
    top_inverse = lower_inverse(lax.linalg.cholesky(top))
    side_factor = mm(side, top_inverse.T)
    schur = bottom - mm(side_factor, side_factor.T)
    schur, carried = lax.optimization_barrier((schur, carried))
    bottom_inverse = lower_inverse(lax.linalg.cholesky(schur))
    corner = -mm(bottom_inverse, mm(side_factor, top_inverse))
    zeros = jnp.zeros((half, matrix.shape[0] - half), matrix.dtype)
    inverse = jnp.concatenate(
        [jnp.concatenate([top_inverse, zeros], 1), jnp.concatenate([corner, bottom_inverse], 1)], 0
    )
    return mm(inverse.T, inverse), carried


def solution(mesh):
    in_specs = (
        P(("tiles", "rep"), None, None),
        P(("tiles", "rep"), None),
        P(("tiles", "rep")),
        P(("tiles", "rep")),
        P(),
        P(("tiles", "rep"), None),
        P(),
    )
    out_specs = P(("tiles", "rep"), None)
    return jax.shard_map(
        per_device, mesh=mesh, in_specs=in_specs, out_specs=out_specs, check_vma=False
    )
```

```python
import jax
import jax.numpy as jnp
from jax import lax
from jax.experimental import pallas as pl
from jax.experimental.pallas import tpu as pltpu
from jax.sharding import PartitionSpec as P


def per_device(tile_data, tile_coords, tile_count, weights, owner_map, factor_b, factor_c):
    slot_total = tile_data.shape[0]
    tile_edge = tile_data.shape[1]
    rank_cols = factor_b.shape[1]
    is_live = jnp.arange(slot_total, dtype=jnp.int32) < tile_count[0]
    slot_scale = weights.astype(jnp.float32) * is_live.astype(jnp.float32)
    stored_second = jnp.take(owner_map, tile_coords[:, 1])
    replicas = lax.psum(1, "rep")
    copies = jnp.broadcast_to(factor_b[None], (replicas,) + factor_b.shape)
    owned = lax.all_to_all(copies, "rep", 0, 0).reshape(-1, rank_cols)
    whole_b = lax.all_gather(owned, "tiles", axis=0, tiled=True)
    inners = []
    b_blocks = []
    for position in range(slot_total):
        c_block = lax.dynamic_slice_in_dim(
            factor_c, tile_coords[position, 2] * tile_edge, tile_edge, 0
        ).astype(jnp.float32)
        b_blocks.append(
            lax.dynamic_slice_in_dim(whole_b, stored_second[position] * tile_edge, tile_edge, 0)
        )
        flat_tile = tile_data[position].reshape(tile_edge * tile_edge, tile_edge)
        inner_sum = jnp.dot(flat_tile, c_block, precision=lax.Precision.HIGHEST)
        inners.append(inner_sum.reshape(tile_edge, tile_edge, rank_cols))
    summed, gram_b = weighted_sum(slot_scale, jnp.stack(b_blocks), whole_b, inners)
    pieces = summed.reshape(replicas, tile_edge // replicas, rank_cols)
    my_rows = lax.all_to_all(pieces, "rep", 0, 0).sum(0)
    gram_c = jnp.dot(factor_c.T, factor_c, preferred_element_type=jnp.float32)
    normal_matrix = gram_b * gram_c
    normal_inverse, my_rows = spd_inverse(normal_matrix, my_rows)
    return jnp.dot(my_rows, normal_inverse, precision=lax.Precision.HIGHEST)


def weigh_kernel(scale_ref, b_ref, whole_ref, *refs):
    inner_refs, out_ref, gram_ref = refs[:-2], refs[-2], refs[-1]
    chunk = whole_ref[...]
    gram_part = lax.dot_general(
        chunk, chunk, (((0,), (0,)), ((), ())), preferred_element_type=jnp.float32
    )

    @pl.when(pl.program_id(0) == 0)
    def _():
        gram_ref[...] = gram_part

    @pl.when(pl.program_id(0) > 0)
    def _():
        gram_ref[...] = gram_ref[...] + gram_part

    total = jnp.zeros(out_ref.shape, jnp.float32)
    for slot, inner_ref in enumerate(inner_refs):
        second = b_ref[slot].astype(jnp.float32)
        partial_value = jnp.sum(inner_ref[...] * second[None], axis=1)
        rounded = (partial_value * scale_ref[slot]).astype(jnp.bfloat16)
        total = total + rounded.astype(jnp.float32)
    out_ref[...] = total


def weighted_sum(slot_scale, b_blocks, whole_b, inners, rows=8):
    edge, second, rank_cols = inners[0].shape
    steps = edge // rows
    inner_spec = pl.BlockSpec((rows, second, rank_cols), lambda i: (i, 0, 0))
    whole_rows = whole_b.shape[0] // steps
    return pl.pallas_call(
        weigh_kernel,
        grid=(steps,),
        in_specs=[
            pl.BlockSpec(memory_space=pltpu.SMEM),
            pl.BlockSpec(b_blocks.shape, lambda i: (0, 0, 0)),
            pl.BlockSpec((whole_rows, rank_cols), lambda i: (i, 0)),
        ]
        + [inner_spec] * len(inners),
        out_specs=[
            pl.BlockSpec((rows, rank_cols), lambda i: (i, 0)),
            pl.BlockSpec((rank_cols, rank_cols), lambda i: (0, 0)),
        ],
        out_shape=[
            jax.ShapeDtypeStruct((edge, rank_cols), jnp.float32),
            jax.ShapeDtypeStruct((rank_cols, rank_cols), jnp.float32),
        ],
    )(slot_scale, b_blocks, whole_b, *inners)


def mm(left, right):
    return jnp.dot(left, right, precision=lax.Precision.HIGHEST)


def lower_inverse(lower):
    size = lower.shape[0]
    identity = jnp.eye(size, dtype=lower.dtype)
    diagonal = jnp.sum(lower * identity, axis=1)
    strict = identity - lower / diagonal[:, None]
    product = identity + strict
    power = strict
    reach = 2
    while reach < size:
        power = mm(power, power)
        product = product + mm(product, power)
        reach *= 2
    return product / diagonal[None, :]


def spd_inverse(matrix, carried):
    half = matrix.shape[0] // 2
    top = matrix[:half, :half]
    side = matrix[half:, :half]
    bottom = matrix[half:, half:]
    top_inverse = lower_inverse(lax.linalg.cholesky(top))
    side_factor = mm(side, top_inverse.T)
    schur = bottom - mm(side_factor, side_factor.T)
    schur, carried = lax.optimization_barrier((schur, carried))
    bottom_inverse = lower_inverse(lax.linalg.cholesky(schur))
    corner = -mm(bottom_inverse, mm(side_factor, top_inverse))
    zeros = jnp.zeros((half, matrix.shape[0] - half), matrix.dtype)
    inverse = jnp.concatenate(
        [jnp.concatenate([top_inverse, zeros], 1), jnp.concatenate([corner, bottom_inverse], 1)], 0
    )
    return mm(inverse.T, inverse), carried


def solution(mesh):
    in_specs = (
        P(("tiles", "rep"), None, None),
        P(("tiles", "rep"), None),
        P(("tiles", "rep")),
        P(("tiles", "rep")),
        P(),
        P(("tiles", "rep"), None),
        P(),
    )
    out_specs = P(("tiles", "rep"), None)
    return jax.shard_map(
        per_device, mesh=mesh, in_specs=in_specs, out_specs=out_specs, check_vma=False
    )
```

```python
import jax
import jax.numpy as jnp
from jax import lax
from jax.experimental import pallas as pl
from jax.experimental.pallas import tpu as pltpu
from jax.sharding import PartitionSpec as P


def per_device(tile_data, tile_coords, tile_count, weights, owner_map, factor_b, factor_c):
    slot_total = tile_data.shape[0]
    tile_edge = tile_data.shape[1]
    rank_cols = factor_b.shape[1]
    is_live = jnp.arange(slot_total, dtype=jnp.int32) < tile_count[0]
    slot_scale = weights.astype(jnp.float32) * is_live.astype(jnp.float32)
    stored_second = jnp.take(owner_map, tile_coords[:, 1])
    replicas = lax.psum(1, "rep")
    copies = jnp.broadcast_to(factor_b[None], (replicas,) + factor_b.shape)
    owned = lax.all_to_all(copies, "rep", 0, 0).reshape(-1, rank_cols)
    whole_b = lax.all_gather(owned, "tiles", axis=0, tiled=True)
    inners = []
    b_blocks = []
    for position in range(slot_total):
        c_block = lax.dynamic_slice_in_dim(
            factor_c, tile_coords[position, 2] * tile_edge, tile_edge, 0
        ).astype(jnp.float32)
        b_blocks.append(
            lax.dynamic_slice_in_dim(whole_b, stored_second[position] * tile_edge, tile_edge, 0)
        )
        flat_tile = tile_data[position].reshape(tile_edge * tile_edge, tile_edge)
        inner_sum = jnp.dot(flat_tile, c_block, precision=lax.Precision.HIGHEST)
        inners.append(inner_sum.reshape(tile_edge, tile_edge, rank_cols))
    summed, gram_b = weighted_sum(slot_scale, jnp.stack(b_blocks), whole_b, inners)
    pieces = summed.reshape(replicas, tile_edge // replicas, rank_cols)
    my_rows = lax.all_to_all(pieces, "rep", 0, 0).sum(0)
    gram_c = jnp.dot(factor_c.T, factor_c, preferred_element_type=jnp.float32)
    normal_matrix = gram_b * gram_c
    normal_inverse, my_rows = spd_inverse(normal_matrix, my_rows)
    return jnp.dot(my_rows, normal_inverse, precision=lax.Precision.HIGHEST)


def weigh_kernel(scale_ref, b_ref, whole_ref, *refs):
    inner_refs, out_ref, gram_ref = refs[:-2], refs[-2], refs[-1]
    chunk = whole_ref[...]
    gram_part = lax.dot_general(
        chunk, chunk, (((0,), (0,)), ((), ())), preferred_element_type=jnp.float32
    )

    @pl.when(pl.program_id(0) == 0)
    def _():
        gram_ref[...] = gram_part

    @pl.when(pl.program_id(0) > 0)
    def _():
        gram_ref[...] = gram_ref[...] + gram_part

    total = jnp.zeros(out_ref.shape, jnp.float32)
    for slot, inner_ref in enumerate(inner_refs):
        second = b_ref[slot].astype(jnp.float32)
        partial_value = jnp.sum(inner_ref[...] * second[None], axis=1)
        rounded = (partial_value * scale_ref[slot]).astype(jnp.bfloat16)
        total = total + rounded.astype(jnp.float32)
    out_ref[...] = total


def weighted_sum(slot_scale, b_blocks, whole_b, inners, rows=32):
    edge, second, rank_cols = inners[0].shape
    steps = edge // rows
    inner_spec = pl.BlockSpec((rows, second, rank_cols), lambda i: (i, 0, 0))
    whole_rows = whole_b.shape[0] // steps
    return pl.pallas_call(
        weigh_kernel,
        grid=(steps,),
        in_specs=[
            pl.BlockSpec(memory_space=pltpu.SMEM),
            pl.BlockSpec(b_blocks.shape, lambda i: (0, 0, 0)),
            pl.BlockSpec((whole_rows, rank_cols), lambda i: (i, 0)),
        ]
        + [inner_spec] * len(inners),
        out_specs=[
            pl.BlockSpec((rows, rank_cols), lambda i: (i, 0)),
            pl.BlockSpec((rank_cols, rank_cols), lambda i: (0, 0)),
        ],
        out_shape=[
            jax.ShapeDtypeStruct((edge, rank_cols), jnp.float32),
            jax.ShapeDtypeStruct((rank_cols, rank_cols), jnp.float32),
        ],
    )(slot_scale, b_blocks, whole_b, *inners)


def mm(left, right):
    return jnp.dot(left, right, precision=lax.Precision.HIGHEST)


def lower_inverse(lower):
    size = lower.shape[0]
    identity = jnp.eye(size, dtype=lower.dtype)
    diagonal = jnp.sum(lower * identity, axis=1)
    strict = identity - lower / diagonal[:, None]
    product = identity + strict
    power = strict
    reach = 2
    while reach < size:
        power = mm(power, power)
        product = product + mm(product, power)
        reach *= 2
    return product / diagonal[None, :]


def spd_inverse(matrix, carried):
    half = matrix.shape[0] // 2
    top = matrix[:half, :half]
    side = matrix[half:, :half]
    bottom = matrix[half:, half:]
    top_inverse = lower_inverse(lax.linalg.cholesky(top))
    side_factor = mm(side, top_inverse.T)
    schur = bottom - mm(side_factor, side_factor.T)
    schur, carried = lax.optimization_barrier((schur, carried))
    bottom_inverse = lower_inverse(lax.linalg.cholesky(schur))
    corner = -mm(bottom_inverse, mm(side_factor, top_inverse))
    zeros = jnp.zeros((half, matrix.shape[0] - half), matrix.dtype)
    inverse = jnp.concatenate(
        [jnp.concatenate([top_inverse, zeros], 1), jnp.concatenate([corner, bottom_inverse], 1)], 0
    )
    return mm(inverse.T, inverse), carried


def solution(mesh):
    in_specs = (
        P(("tiles", "rep"), None, None),
        P(("tiles", "rep"), None),
        P(("tiles", "rep")),
        P(("tiles", "rep")),
        P(),
        P(("tiles", "rep"), None),
        P(),
    )
    out_specs = P(("tiles", "rep"), None)
    return jax.shard_map(
        per_device, mesh=mesh, in_specs=in_specs, out_specs=out_specs, check_vma=False
    )
```

```python
import jax
import jax.numpy as jnp
from jax import lax
from jax.experimental import pallas as pl
from jax.experimental.pallas import tpu as pltpu
from jax.sharding import PartitionSpec as P


def per_device(tile_data, tile_coords, tile_count, weights, owner_map, factor_b, factor_c):
    slot_total = tile_data.shape[0]
    tile_edge = tile_data.shape[1]
    rank_cols = factor_b.shape[1]
    is_live = jnp.arange(slot_total, dtype=jnp.int32) < tile_count[0]
    slot_scale = weights.astype(jnp.float32) * is_live.astype(jnp.float32)
    stored_second = jnp.take(owner_map, tile_coords[:, 1])
    replicas = lax.psum(1, "rep")
    copies = jnp.broadcast_to(factor_b[None], (replicas,) + factor_b.shape)
    owned = lax.all_to_all(copies, "rep", 0, 0).reshape(-1, rank_cols)
    whole_b = lax.all_gather(owned, "tiles", axis=0, tiled=True)
    inners = []
    b_blocks = []
    for position in range(slot_total):
        c_block = lax.dynamic_slice_in_dim(
            factor_c, tile_coords[position, 2] * tile_edge, tile_edge, 0
        ).astype(jnp.float32)
        b_blocks.append(
            lax.dynamic_slice_in_dim(whole_b, stored_second[position] * tile_edge, tile_edge, 0)
        )
        flat_tile = tile_data[position].reshape(tile_edge * tile_edge, tile_edge)
        inner_sum = jnp.dot(flat_tile, c_block, precision=lax.Precision.HIGHEST)
        inners.append(inner_sum.reshape(tile_edge, tile_edge, rank_cols))
    summed, gram_b = weighted_sum(slot_scale, jnp.stack(b_blocks), whole_b, inners)
    pieces = summed.reshape(replicas, tile_edge // replicas, rank_cols)
    my_rows = lax.all_to_all(pieces, "rep", 0, 0).sum(0)
    gram_c = jnp.dot(factor_c.T, factor_c, preferred_element_type=jnp.float32)
    normal_matrix = gram_b * gram_c
    normal_inverse, my_rows = spd_inverse(normal_matrix, my_rows)
    return jnp.dot(my_rows, normal_inverse, precision=lax.Precision.HIGHEST)


def weigh_kernel(scale_ref, b_ref, whole_ref, *refs):
    inner_refs, out_ref, gram_ref = refs[:-2], refs[-2], refs[-1]
    chunk = whole_ref[...]
    gram_part = lax.dot_general(
        chunk, chunk, (((0,), (0,)), ((), ())), preferred_element_type=jnp.float32
    )

    @pl.when(pl.program_id(0) == 0)
    def _():
        gram_ref[...] = gram_part

    @pl.when(pl.program_id(0) > 0)
    def _():
        gram_ref[...] = gram_ref[...] + gram_part

    total = jnp.zeros(out_ref.shape, jnp.float32)
    for slot, inner_ref in enumerate(inner_refs):
        second = b_ref[slot].astype(jnp.float32)
        weighed = inner_ref[...] * second[None]
        rows, width, rank_cols = weighed.shape
        partial_value = weighed.reshape(rows, width // 8, 8, rank_cols).sum(axis=1).sum(axis=1)
        rounded = (partial_value * scale_ref[slot]).astype(jnp.bfloat16)
        total = total + rounded.astype(jnp.float32)
    out_ref[...] = total


def weighted_sum(slot_scale, b_blocks, whole_b, inners, rows=32):
    edge, second, rank_cols = inners[0].shape
    steps = edge // rows
    inner_spec = pl.BlockSpec((rows, second, rank_cols), lambda i: (i, 0, 0))
    whole_rows = whole_b.shape[0] // steps
    return pl.pallas_call(
        weigh_kernel,
        grid=(steps,),
        in_specs=[
            pl.BlockSpec(memory_space=pltpu.SMEM),
            pl.BlockSpec(b_blocks.shape, lambda i: (0, 0, 0)),
            pl.BlockSpec((whole_rows, rank_cols), lambda i: (i, 0)),
        ]
        + [inner_spec] * len(inners),
        out_specs=[
            pl.BlockSpec((rows, rank_cols), lambda i: (i, 0)),
            pl.BlockSpec((rank_cols, rank_cols), lambda i: (0, 0)),
        ],
        out_shape=[
            jax.ShapeDtypeStruct((edge, rank_cols), jnp.float32),
            jax.ShapeDtypeStruct((rank_cols, rank_cols), jnp.float32),
        ],
    )(slot_scale, b_blocks, whole_b, *inners)


def mm(left, right):
    return jnp.dot(left, right, precision=lax.Precision.HIGHEST)


def lower_inverse(lower):
    size = lower.shape[0]
    identity = jnp.eye(size, dtype=lower.dtype)
    diagonal = jnp.sum(lower * identity, axis=1)
    strict = identity - lower / diagonal[:, None]
    product = identity + strict
    power = strict
    reach = 2
    while reach < size:
        power = mm(power, power)
        product = product + mm(product, power)
        reach *= 2
    return product / diagonal[None, :]


def spd_inverse(matrix, carried):
    half = matrix.shape[0] // 2
    top = matrix[:half, :half]
    side = matrix[half:, :half]
    bottom = matrix[half:, half:]
    top_inverse = lower_inverse(lax.linalg.cholesky(top, symmetrize_input=False))
    side_factor = mm(side, top_inverse.T)
    schur = bottom - mm(side_factor, side_factor.T)
    schur, carried = lax.optimization_barrier((schur, carried))
    bottom_inverse = lower_inverse(lax.linalg.cholesky(schur, symmetrize_input=False))
    corner = -mm(bottom_inverse, mm(side_factor, top_inverse))
    zeros = jnp.zeros((half, matrix.shape[0] - half), matrix.dtype)
    inverse = jnp.concatenate(
        [jnp.concatenate([top_inverse, zeros], 1), jnp.concatenate([corner, bottom_inverse], 1)], 0
    )
    return mm(inverse.T, inverse), carried


def solution(mesh):
    in_specs = (
        P(("tiles", "rep"), None, None),
        P(("tiles", "rep"), None),
        P(("tiles", "rep")),
        P(("tiles", "rep")),
        P(),
        P(("tiles", "rep"), None),
        P(),
    )
    out_specs = P(("tiles", "rep"), None)
    return jax.shard_map(
        per_device, mesh=mesh, in_specs=in_specs, out_specs=out_specs, check_vma=False
    )
```

```python
import jax
import jax.numpy as jnp
from jax import lax
from jax.experimental import pallas as pl
from jax.experimental.pallas import tpu as pltpu
from jax.sharding import PartitionSpec as P


def per_device(tile_data, tile_coords, tile_count, weights, owner_map, factor_b, factor_c):
    slot_total = tile_data.shape[0]
    tile_edge = tile_data.shape[1]
    rank_cols = factor_b.shape[1]
    is_live = jnp.arange(slot_total, dtype=jnp.int32) < tile_count[0]
    slot_scale = weights.astype(jnp.float32) * is_live.astype(jnp.float32)
    stored_second = jnp.take(owner_map, tile_coords[:, 1])
    replicas = lax.psum(1, "rep")
    copies = jnp.broadcast_to(factor_b[None], (replicas,) + factor_b.shape)
    owned = lax.all_to_all(copies, "rep", 0, 0).reshape(-1, rank_cols)
    whole_b = lax.all_gather(owned, "tiles", axis=0, tiled=True)
    inners = []
    for position in range(slot_total):
        c_block = lax.dynamic_slice_in_dim(
            factor_c, tile_coords[position, 2] * tile_edge, tile_edge, 0
        ).astype(jnp.float32)
        flat_tile = tile_data[position].reshape(tile_edge * tile_edge, tile_edge)
        inner_sum = jnp.dot(flat_tile, c_block, precision=lax.Precision.HIGHEST)
        inners.append(inner_sum.reshape(tile_edge, tile_edge, rank_cols))
    summed, gram_b = weighted_sum(stored_second, slot_scale, whole_b, inners)
    pieces = summed.reshape(replicas, tile_edge // replicas, rank_cols)
    my_rows = lax.all_to_all(pieces, "rep", 0, 0).sum(0)
    gram_c = jnp.dot(factor_c.T, factor_c, preferred_element_type=jnp.float32)
    normal_matrix = gram_b * gram_c
    normal_inverse, my_rows = spd_inverse(normal_matrix, my_rows)
    return jnp.dot(my_rows, normal_inverse, precision=lax.Precision.HIGHEST)


def weigh_kernel(place_ref, scale_ref, whole_ref, *refs):
    del place_ref
    slots = (len(refs) - 2) // 2
    b_refs, inner_refs = refs[:slots], refs[slots:-2]
    out_ref, gram_ref = refs[-2], refs[-1]
    chunk = whole_ref[...]
    gram_part = lax.dot_general(
        chunk, chunk, (((0,), (0,)), ((), ())), preferred_element_type=jnp.float32
    )

    @pl.when(pl.program_id(0) == 0)
    def _():
        gram_ref[...] = gram_part

    @pl.when(pl.program_id(0) > 0)
    def _():
        gram_ref[...] = gram_ref[...] + gram_part

    total = jnp.zeros(out_ref.shape, jnp.float32)
    for slot, inner_ref in enumerate(inner_refs):
        second = b_refs[slot][...].astype(jnp.float32)
        weighed = inner_ref[...] * second[None]
        rows, width, rank_cols = weighed.shape
        partial_value = weighed.reshape(rows, width // 8, 8, rank_cols).sum(axis=1).sum(axis=1)
        rounded = (partial_value * scale_ref[slot]).astype(jnp.bfloat16)
        total = total + rounded.astype(jnp.float32)
    out_ref[...] = total


def weighted_sum(place, slot_scale, whole_b, inners, rows=32):
    edge, second, rank_cols = inners[0].shape
    steps = edge // rows
    whole_rows = whole_b.shape[0] // steps
    b_specs = [
        pl.BlockSpec((second, rank_cols), lambda i, place_ref, slot=slot: (place_ref[slot], 0))
        for slot in range(len(inners))
    ]
    grid_spec = pltpu.PrefetchScalarGridSpec(
        num_scalar_prefetch=1,
        grid=(steps,),
        in_specs=[
            pl.BlockSpec(memory_space=pltpu.SMEM),
            pl.BlockSpec((whole_rows, rank_cols), lambda i, place_ref: (i, 0)),
        ]
        + b_specs
        + [pl.BlockSpec((rows, second, rank_cols), lambda i, place_ref: (i, 0, 0))] * len(inners),
        out_specs=[
            pl.BlockSpec((rows, rank_cols), lambda i, place_ref: (i, 0)),
            pl.BlockSpec((rank_cols, rank_cols), lambda i, place_ref: (0, 0)),
        ],
    )
    return pl.pallas_call(
        weigh_kernel,
        grid_spec=grid_spec,
        out_shape=[
            jax.ShapeDtypeStruct((edge, rank_cols), jnp.float32),
            jax.ShapeDtypeStruct((rank_cols, rank_cols), jnp.float32),
        ],
    )(place, slot_scale, whole_b, *([whole_b] * len(inners)), *inners)


def mm(left, right):
    return jnp.dot(left, right, precision=lax.Precision.HIGHEST)


def lower_inverse(lower):
    size = lower.shape[0]
    identity = jnp.eye(size, dtype=lower.dtype)
    diagonal = jnp.sum(lower * identity, axis=1)
    strict = identity - lower / diagonal[:, None]
    product = identity + strict
    power = strict
    reach = 2
    while reach < size:
        power = mm(power, power)
        product = product + mm(product, power)
        reach *= 2
    return product / diagonal[None, :]


def spd_inverse(matrix, carried):
    half = matrix.shape[0] // 2
    top = matrix[:half, :half]
    side = matrix[half:, :half]
    bottom = matrix[half:, half:]
    top_inverse = lower_inverse(lax.linalg.cholesky(top, symmetrize_input=False))
    side_factor = mm(side, top_inverse.T)
    schur = bottom - mm(side_factor, side_factor.T)
    schur, carried = lax.optimization_barrier((schur, carried))
    bottom_inverse = lower_inverse(lax.linalg.cholesky(schur, symmetrize_input=False))
    corner = -mm(bottom_inverse, mm(side_factor, top_inverse))
    zeros = jnp.zeros((half, matrix.shape[0] - half), matrix.dtype)
    inverse = jnp.concatenate(
        [jnp.concatenate([top_inverse, zeros], 1), jnp.concatenate([corner, bottom_inverse], 1)], 0
    )
    return mm(inverse.T, inverse), carried


def solution(mesh):
    in_specs = (
        P(("tiles", "rep"), None, None),
        P(("tiles", "rep"), None),
        P(("tiles", "rep")),
        P(("tiles", "rep")),
        P(),
        P(("tiles", "rep"), None),
        P(),
    )
    out_specs = P(("tiles", "rep"), None)
    return jax.shard_map(
        per_device, mesh=mesh, in_specs=in_specs, out_specs=out_specs, check_vma=False
    )
```

```python
import jax
import jax.numpy as jnp
from jax import lax
from jax.experimental import pallas as pl
from jax.experimental.pallas import tpu as pltpu
from jax.sharding import PartitionSpec as P


def per_device(tile_data, tile_coords, tile_count, weights, owner_map, factor_b, factor_c):
    slot_total = tile_data.shape[0]
    tile_edge = tile_data.shape[1]
    rank_cols = factor_b.shape[1]
    is_live = jnp.arange(slot_total, dtype=jnp.int32) < tile_count[0]
    slot_scale = weights.astype(jnp.float32) * is_live.astype(jnp.float32)
    stored_second = jnp.take(owner_map, tile_coords[:, 1])
    replicas = lax.psum(1, "rep")
    copies = jnp.broadcast_to(factor_b[None], (replicas,) + factor_b.shape)
    owned = lax.all_to_all(copies, "rep", 0, 0).reshape(-1, rank_cols)
    whole_b = lax.all_gather(owned, "tiles", axis=0, tiled=True)
    inners = []
    for position in range(slot_total):
        c_block = lax.dynamic_slice_in_dim(
            factor_c, tile_coords[position, 2] * tile_edge, tile_edge, 0
        ).astype(jnp.float32)
        flat_tile = tile_data[position].reshape(tile_edge * tile_edge, tile_edge)
        inner_sum = jnp.dot(flat_tile, c_block, precision=lax.Precision.HIGHEST)
        inners.append(inner_sum.reshape(tile_edge, tile_edge, rank_cols))
    summed, gram_b = weighted_sum(stored_second, slot_scale, whole_b, inners)
    pieces = summed.reshape(replicas, tile_edge // replicas, rank_cols)
    my_rows = lax.all_to_all(pieces, "rep", 0, 0).sum(0)
    gram_c = jnp.dot(factor_c.T, factor_c, preferred_element_type=jnp.float32)
    normal_matrix = gram_b * gram_c
    lower_inv, my_rows = spd_inverse(normal_matrix, my_rows)
    return mm(mm(my_rows, lower_inv.T), lower_inv)


def weigh_kernel(place_ref, scale_ref, whole_ref, *refs):
    del place_ref
    slots = (len(refs) - 2) // 2
    b_refs, inner_refs = refs[:slots], refs[slots:-2]
    out_ref, gram_ref = refs[-2], refs[-1]
    chunk = whole_ref[...]
    gram_part = lax.dot_general(
        chunk, chunk, (((0,), (0,)), ((), ())), preferred_element_type=jnp.float32
    )

    @pl.when(pl.program_id(0) == 0)
    def _():
        gram_ref[...] = gram_part

    @pl.when(pl.program_id(0) > 0)
    def _():
        gram_ref[...] = gram_ref[...] + gram_part

    total = jnp.zeros(out_ref.shape, jnp.float32)
    for slot, inner_ref in enumerate(inner_refs):
        second = b_refs[slot][...].astype(jnp.float32)
        weighed = inner_ref[...] * second[None]
        rows, width, rank_cols = weighed.shape
        partial_value = weighed.reshape(rows, width // 8, 8, rank_cols).sum(axis=1).sum(axis=1)
        rounded = (partial_value * scale_ref[slot]).astype(jnp.bfloat16)
        total = total + rounded.astype(jnp.float32)
    out_ref[...] = total


def weighted_sum(place, slot_scale, whole_b, inners, rows=32):
    edge, second, rank_cols = inners[0].shape
    steps = edge // rows
    whole_rows = whole_b.shape[0] // steps
    b_specs = [
        pl.BlockSpec((second, rank_cols), lambda i, place_ref, slot=slot: (place_ref[slot], 0))
        for slot in range(len(inners))
    ]
    grid_spec = pltpu.PrefetchScalarGridSpec(
        num_scalar_prefetch=1,
        grid=(steps,),
        in_specs=[
            pl.BlockSpec(memory_space=pltpu.SMEM),
            pl.BlockSpec((whole_rows, rank_cols), lambda i, place_ref: (i, 0)),
        ]
        + b_specs
        + [pl.BlockSpec((rows, second, rank_cols), lambda i, place_ref: (i, 0, 0))] * len(inners),
        out_specs=[
            pl.BlockSpec((rows, rank_cols), lambda i, place_ref: (i, 0)),
            pl.BlockSpec((rank_cols, rank_cols), lambda i, place_ref: (0, 0)),
        ],
    )
    return pl.pallas_call(
        weigh_kernel,
        grid_spec=grid_spec,
        out_shape=[
            jax.ShapeDtypeStruct((edge, rank_cols), jnp.float32),
            jax.ShapeDtypeStruct((rank_cols, rank_cols), jnp.float32),
        ],
    )(place, slot_scale, whole_b, *([whole_b] * len(inners)), *inners)


def mm(left, right):
    return jnp.dot(left, right, precision=lax.Precision.HIGHEST)


def lower_inverse(lower):
    size = lower.shape[0]
    identity = jnp.eye(size, dtype=lower.dtype)
    diagonal = jnp.sum(lower * identity, axis=1)
    strict = identity - lower / diagonal[:, None]
    product = identity + strict
    power = strict
    reach = 2
    while reach < size:
        power = mm(power, power)
        product = product + mm(product, power)
        reach *= 2
    return product / diagonal[None, :]


def spd_inverse(matrix, carried):
    half = matrix.shape[0] // 2
    top = matrix[:half, :half]
    side = matrix[half:, :half]
    bottom = matrix[half:, half:]
    top_inverse = lower_inverse(lax.linalg.cholesky(top, symmetrize_input=False))
    side_factor = mm(side, top_inverse.T)
    schur = bottom - mm(side_factor, side_factor.T)
    schur, carried = lax.optimization_barrier((schur, carried))
    bottom_inverse = lower_inverse(lax.linalg.cholesky(schur, symmetrize_input=False))
    corner = -mm(bottom_inverse, mm(side_factor, top_inverse))
    zeros = jnp.zeros((half, matrix.shape[0] - half), matrix.dtype)
    inverse = jnp.concatenate(
        [jnp.concatenate([top_inverse, zeros], 1), jnp.concatenate([corner, bottom_inverse], 1)], 0
    )
    return inverse, carried


def solution(mesh):
    in_specs = (
        P(("tiles", "rep"), None, None),
        P(("tiles", "rep"), None),
        P(("tiles", "rep")),
        P(("tiles", "rep")),
        P(),
        P(("tiles", "rep"), None),
        P(),
    )
    out_specs = P(("tiles", "rep"), None)
    return jax.shard_map(
        per_device, mesh=mesh, in_specs=in_specs, out_specs=out_specs, check_vma=False
    )
```
